512 devices in a mesh: row: 32 (over y_lo, z), col: 16 (over y_hi, x, core).
Axes of the slice: x: 4, y: 8 (y_hi: 2, y_lo: 4; y = y_hi * 4 + y_lo), z: 8, core: 2. Of those that a mesh axis runs over, the one named last changes fastest.
Arguments:
- upper: float32 [8192, 8192], P('row', 'col'), may hold values from -0.125 to 0.125
- occupied: int32 [64, 64], P('row', 'col'), may hold values 0 or 1
- tile_molecules: int32 [64], replicated, may hold values from 2 to 5
Outputs:
- square_part: float32 [8192, 8192], P('row', 'col')
The draws below stay inside these ranges and needn't reach their ends.
Inputs may be any that keep to these rules, and one draw needn't show every extreme that they name: `occupied`: only entries with row below column are read.
All inputs are finite; a program needn't handle non-finite values. No bound on the sum of `occupied` on one device may be relied on, other than what follows from the above.
Results may differ from the reference program's by a relative error of at most 0.0003.
Values sent between devices are 32-bit elements; how exact they have to be, the bound alone decides.
No kernel may reach another device: no remote copies, remote signals or barrier semaphores. Data moves between devices by JAX's collectives and lax.ppermute only.
A program may use at most 64 MiB of HBM per device.

```python
import jax
import jax.numpy as jnp
from jax import lax

BASIS = 23
MOL_MAX = 5
TILE = 128
TR = 2
STEPS = 14
NB = 64
ORDER = 8192
N_ROW = 32
N_COL = 16


def plant(values, own_key, low, top_value):
    dims = values.shape
    place = [jax.random.randint(jax.random.fold_in(own_key, axis), (), 0, dims[axis]) for axis in range(len(dims))]
    values = values.at[tuple(place)].set(low)
    longest = dims.index(max(dims))
    place[longest] = (place[longest] + 1) % dims[longest]
    return values.at[tuple(place)].set(top_value)


def shard_levels(own_key, shape, cuts, smallest, largest):
    def one(position, blocks):
        draws = jax.random.uniform(jax.random.fold_in(jax.random.fold_in(own_key, 6), position), (blocks,), jnp.float32, smallest / len(cuts), largest / len(cuts))
        return jnp.repeat(jnp.exp(draws), shape[position] // blocks).reshape((-1,) + (1,) * (len(shape) - position - 1))

    gain = one(*cuts[0])
    for cut in cuts[1:]:
        gain = gain * one(*cut)
    return gain


def normal_values(stream_key, shape, scale, bound, split=(), held_as=jnp.bfloat16):
    entries = scale * jax.random.normal(stream_key, shape, jnp.float32)
    if split:
        entries = entries * shard_levels(stream_key, shape, split, -0.22, 0.18)
    return jnp.clip(entries, -bound, bound).astype(held_as)


def setup_inputs(seed: int = 0) -> dict:
    key_list = jax.random.split(jax.random.key(seed), 4)
    upper = normal_values(key_list[0], (ORDER, ORDER), (TILE * TR * STEPS // 2) ** -0.5, 0.125, ((0, 32), (1, 16)), jnp.float32)
    occupied = plant((jax.random.randint(key_list[1], (NB, NB), 0, 2) < 1).astype(jnp.int32), jax.random.fold_in(key_list[1], 1), 0, 1)
    tile_molecules = plant(jax.random.randint(key_list[2], (NB,), 2, MOL_MAX + 1), jax.random.fold_in(key_list[2], 1), 2, MOL_MAX).astype(jnp.int32)
    return {"upper": upper, "occupied": occupied, "tile_molecules": tile_molecules}


def reference(upper, occupied, tile_molecules):
    blocks_count = TR * N_ROW
    height = TR * TILE
    tiles = jnp.arange(blocks_count)
    factor = jnp.where(tiles[:, None] < tiles[None, :], occupied.astype(jnp.float32),
                       jnp.where(tiles[:, None] == tiles[None, :], 0.5, 0.0)).astype(jnp.float32)
    half_tri = (upper.reshape(blocks_count, TILE, blocks_count, TILE) * factor[:, None, :, None]).reshape(blocks_count * TILE, blocks_count * TILE)
    live = (jnp.arange(TILE)[None, :] < BASIS * tile_molecules[:, None]).astype(jnp.float32).reshape(-1)
    density = (half_tri + half_tri.T) * live[:, None] * live[None, :]
    blocks = density.reshape(N_ROW, height, N_ROW, height)
    columns = density.reshape(N_ROW, height, N_COL, 2 * height)
    col_ids = jnp.arange(N_COL)

    def one_row(row_group):
        row_blocks = blocks[row_group]

        def one_step(total, step):
            kappa = (row_group + 2 * col_ids + step) % N_ROW
            left = row_blocks[:, kappa, :]
            right = columns[kappa, :, col_ids, :]
            term = jnp.einsum("ack,ckj->caj", left, right, precision=lax.Precision.HIGHEST)
            return total + term, None

        start = jnp.zeros((N_COL, height, 2 * height), jnp.float32)
        total, _ = lax.scan(one_step, start, jnp.arange(STEPS))
        return total

    result = lax.map(one_row, jnp.arange(N_ROW))
    return result.transpose(0, 2, 1, 3).reshape(blocks_count * TILE, blocks_count * TILE)
```

```python
import jax
import jax.numpy as jnp
from jax import lax
from jax.sharding import PartitionSpec as P

BASIS = 23
TILE = 128
TR = 2
STEPS = 14

AXES = ("row", "col")


def send(value, pairs):
    return lax.ppermute(value, AXES, pairs)


def mirror_pairs(row_count, col_count, flip):
    pairs = []
    for r in range(row_count):
        for c in range(col_count):
            half = (r % 2) ^ flip
            target = (2 * c + half, r // 2)
            pairs.append((r * col_count + c, target[0] * col_count + target[1]))
    return pairs


def left_pairs(row_count, col_count, step):
    pairs = []
    for r in range(row_count):
        half = (r + step) % 2
        for c in range(col_count):
            target = ((2 * c + half - r - step) % row_count) // 2
            pairs.append((r * col_count + c, r * col_count + target))
    return pairs


def right_pairs(row_count, col_count, step):
    pairs = []
    for r in range(row_count):
        for c in range(col_count):
            target = (r - 2 * c - step) % row_count
            pairs.append((r * col_count + c, target * col_count + c))
    return pairs


def body(upper, occupied, tile_molecules):
    row_id = lax.axis_index("row")
    col_id = lax.axis_index("col")
    row_count = lax.axis_size("row")
    col_count = lax.axis_size("col")
    height = upper.shape[0]
    width = upper.shape[1]
    half_width = width // 2
    row_tiles = row_id * TR + jnp.arange(TR, dtype=jnp.int32)
    col_tiles = col_id * (2 * TR) + jnp.arange(2 * TR, dtype=jnp.int32)
    factor = jnp.where(
        row_tiles[:, None] < col_tiles[None, :],
        occupied.astype(jnp.float32),
        jnp.where(row_tiles[:, None] == col_tiles[None, :], 0.5, 0.0),
    )
    half_tri = (upper.reshape(TR, TILE, 2 * TR, TILE) * factor[:, None, :, None]).reshape(
        height, width
    )
    parity = row_id % 2
    halves = half_tri.reshape(height, 2, half_width)
    own_half = jnp.where(parity == 0, halves[:, 0], halves[:, 1]).T
    other_half = jnp.where(parity == 0, halves[:, 1], halves[:, 0]).T
    got_same = send(own_half, mirror_pairs(row_count, col_count, 0))
    got_other = send(other_half, mirror_pairs(row_count, col_count, 1))
    mirrored = jnp.where(
        parity == 0,
        jnp.concatenate([got_same, got_other], axis=1),
        jnp.concatenate([got_other, got_same], axis=1),
    )
    mol_rows = lax.dynamic_slice_in_dim(tile_molecules, row_id * TR, TR)
    mol_cols = lax.dynamic_slice_in_dim(tile_molecules, col_id * (2 * TR), 2 * TR)
    offsets = jnp.arange(TILE, dtype=jnp.int32)
    live_rows = (offsets[None, :] < BASIS * mol_rows[:, None]).astype(jnp.float32).reshape(height)
    live_cols = (offsets[None, :] < BASIS * mol_cols[:, None]).astype(jnp.float32).reshape(width)
    density = (half_tri + mirrored) * live_rows[:, None] * live_cols[None, :]
    dense_halves = density.reshape(height, 2, half_width)
    even_half = dense_halves[:, 0]
    odd_half = dense_halves[:, 1]
    total = None
    for step in range(STEPS):
        piece = jnp.where((row_id + step) % 2 == 0, even_half, odd_half)
        left = send(piece, left_pairs(row_count, col_count, step))
        right = send(density, right_pairs(row_count, col_count, step))
        term = jnp.dot(left, right, precision=lax.Precision.HIGHEST, preferred_element_type=jnp.float32)
        total = term if total is None else total + term
    return total


def solution(mesh):
    placed = (P("row", "col"), P("row", "col"), P())
    return jax.shard_map(
        body, mesh=mesh, in_specs=placed, out_specs=P("row", "col"), check_vma=False
    )
```

```python
import jax
import jax.numpy as jnp
from jax import lax
from jax.sharding import PartitionSpec as P

BASIS = 23
TILE = 128
TR = 2
STEPS = 14

AXES = ("row", "col")


def send(value, pairs):
    return lax.ppermute(value, AXES, pairs)


def mirror_pairs(row_count, col_count, flip):
    pairs = []
    for r in range(row_count):
        for c in range(col_count):
            half = (r % 2) ^ flip
            target = (2 * c + half, r // 2)
            pairs.append((r * col_count + c, target[0] * col_count + target[1]))
    return pairs


def body(upper, occupied, tile_molecules):
    row_id = lax.axis_index("row")
    col_id = lax.axis_index("col")
    row_count = lax.axis_size("row")
    col_count = lax.axis_size("col")
    height = upper.shape[0]
    width = upper.shape[1]
    half_width = width // 2
    row_tiles = row_id * TR + jnp.arange(TR, dtype=jnp.int32)
    col_tiles = col_id * (2 * TR) + jnp.arange(2 * TR, dtype=jnp.int32)
    factor = jnp.where(
        row_tiles[:, None] < col_tiles[None, :],
        occupied.astype(jnp.float32),
        jnp.where(row_tiles[:, None] == col_tiles[None, :], 0.5, 0.0),
    )
    half_tri = (upper.reshape(TR, TILE, 2 * TR, TILE) * factor[:, None, :, None]).reshape(
        height, width
    )
    parity = row_id % 2
    halves = half_tri.reshape(height, 2, half_width)
    own_half = jnp.where(parity == 0, halves[:, 0], halves[:, 1]).T
    other_half = jnp.where(parity == 0, halves[:, 1], halves[:, 0]).T
    got_same = send(own_half, mirror_pairs(row_count, col_count, 0))
    got_other = send(other_half, mirror_pairs(row_count, col_count, 1))
    mirrored = jnp.where(
        parity == 0,
        jnp.concatenate([got_same, got_other], axis=1),
        jnp.concatenate([got_other, got_same], axis=1),
    )
    mol_rows = lax.dynamic_slice_in_dim(tile_molecules, row_id * TR, TR)
    mol_cols = lax.dynamic_slice_in_dim(tile_molecules, col_id * (2 * TR), 2 * TR)
    offsets = jnp.arange(TILE, dtype=jnp.int32)
    live_rows = (offsets[None, :] < BASIS * mol_rows[:, None]).astype(jnp.float32).reshape(height)
    live_cols = (offsets[None, :] < BASIS * mol_cols[:, None]).astype(jnp.float32).reshape(width)
    density = (half_tri + mirrored) * live_rows[:, None] * live_cols[None, :]
    row_panel = lax.all_gather(density, "col", axis=1, tiled=True)
    col_panel = lax.all_gather(density, "row", axis=0, tiled=True)
    group = upper.shape[0]
    total = None
    for step in range(STEPS):
        start = (row_id + 2 * col_id + step) % row_count
        left = lax.dynamic_slice_in_dim(row_panel, start * group, group, axis=1)
        right = lax.dynamic_slice_in_dim(col_panel, start * group, group, axis=0)
        term = jnp.dot(left, right, precision=lax.Precision.HIGHEST, preferred_element_type=jnp.float32)
        total = term if total is None else total + term
    return total


def solution(mesh):
    placed = (P("row", "col"), P("row", "col"), P())
    return jax.shard_map(
        body, mesh=mesh, in_specs=placed, out_specs=P("row", "col"), check_vma=False
    )
```

```python
import jax
import jax.numpy as jnp
from jax import lax
from jax.sharding import PartitionSpec as P

BASIS = 23
TILE = 128
TR = 2
STEPS = 14

AXES = ("row", "col")


def send(value, pairs):
    return lax.ppermute(value, AXES, pairs)


def mirror_pairs(row_count, col_count, flip):
    pairs = []
    for r in range(row_count):
        for c in range(col_count):
            half = (r % 2) ^ flip
            target = (2 * c + half, r // 2)
            pairs.append((r * col_count + c, target[0] * col_count + target[1]))
    return pairs


def shift(value, axis, by):
    length = lax.axis_size(axis)
    return lax.ppermute(value, axis, [(i, (i - by) % length) for i in range(length)])


def left_pairs(row_count, col_count, step):
    pairs = []
    for r in range(row_count):
        half = (r + step) % 2
        for c in range(col_count):
            target = ((2 * c + half - r - step) % row_count) // 2
            pairs.append((r * col_count + c, r * col_count + target))
    return pairs


def right_pairs(row_count, col_count, step):
    pairs = []
    for r in range(row_count):
        for c in range(col_count):
            target = (r - 2 * c - step) % row_count
            pairs.append((r * col_count + c, target * col_count + c))
    return pairs


def body(upper, occupied, tile_molecules):
    row_id = lax.axis_index("row")
    col_id = lax.axis_index("col")
    row_count = lax.axis_size("row")
    col_count = lax.axis_size("col")
    height = upper.shape[0]
    width = upper.shape[1]
    half_width = width // 2
    row_tiles = row_id * TR + jnp.arange(TR, dtype=jnp.int32)
    col_tiles = col_id * (2 * TR) + jnp.arange(2 * TR, dtype=jnp.int32)
    factor = jnp.where(
        row_tiles[:, None] < col_tiles[None, :],
        occupied.astype(jnp.float32),
        jnp.where(row_tiles[:, None] == col_tiles[None, :], 0.5, 0.0),
    )
    half_tri = (upper.reshape(TR, TILE, 2 * TR, TILE) * factor[:, None, :, None]).reshape(
        height, width
    )
    parity = row_id % 2
    halves = half_tri.reshape(height, 2, half_width)
    own_half = jnp.where(parity == 0, halves[:, 0], halves[:, 1]).T
    other_half = jnp.where(parity == 0, halves[:, 1], halves[:, 0]).T
    got_same = send(own_half, mirror_pairs(row_count, col_count, 0))
    got_other = send(other_half, mirror_pairs(row_count, col_count, 1))
    mirrored = jnp.where(
        parity == 0,
        jnp.concatenate([got_same, got_other], axis=1),
        jnp.concatenate([got_other, got_same], axis=1),
    )
    mol_rows = lax.dynamic_slice_in_dim(tile_molecules, row_id * TR, TR)
    mol_cols = lax.dynamic_slice_in_dim(tile_molecules, col_id * (2 * TR), 2 * TR)
    offsets = jnp.arange(TILE, dtype=jnp.int32)
    live_rows = (offsets[None, :] < BASIS * mol_rows[:, None]).astype(jnp.float32).reshape(height)
    live_cols = (offsets[None, :] < BASIS * mol_cols[:, None]).astype(jnp.float32).reshape(width)
    density = (half_tri + mirrored) * live_rows[:, None] * live_cols[None, :]
    group = upper.shape[0]
    right = send(density, right_pairs(row_count, col_count, 0))
    have = 1
    while have < STEPS:
        take = min(have, STEPS - have)
        right = jnp.concatenate([right, shift(right[: take * group], "row", have)], axis=0)
        have += take
    dense_halves = density.reshape(height, 2, half_width)
    pieces = []
    for step in range(2):
        piece = jnp.where((row_id + step) % 2 == 0, dense_halves[:, 0], dense_halves[:, 1])
        pieces.append(send(piece, left_pairs(row_count, col_count, step)))
    left = jnp.concatenate(pieces, axis=1)
    have = 2
    while have < STEPS:
        take = min(have, STEPS - have)
        left = jnp.concatenate([left, shift(left[:, : take * group], "col", have // 2)], axis=1)
        have += take
    total = jnp.dot(left, right, precision=lax.Precision.HIGHEST, preferred_element_type=jnp.float32)
    return total


def solution(mesh):
    placed = (P("row", "col"), P("row", "col"), P())
    return jax.shard_map(
        body, mesh=mesh, in_specs=placed, out_specs=P("row", "col"), check_vma=False
    )
```

```python
import jax
import jax.numpy as jnp
from jax import lax
from jax.sharding import PartitionSpec as P

BASIS = 23
TILE = 128
TR = 2
STEPS = 14

AXES = ("row", "col")


def send(value, pairs):
    return lax.ppermute(value, AXES, pairs)


def mirror_pairs(row_count, col_count, flip):
    pairs = []
    for r in range(row_count):
        for c in range(col_count):
            half = (r % 2) ^ flip
            target = (2 * c + half, r // 2)
            pairs.append((r * col_count + c, target[0] * col_count + target[1]))
    return pairs


def shift(value, axis, by):
    length = lax.axis_size(axis)
    return lax.ppermute(value, axis, [(i, (i - by) % length) for i in range(length)])


def left_pairs(row_count, col_count, step):
    pairs = []
    for r in range(row_count):
        half = (r + step) % 2
        for c in range(col_count):
            target = ((2 * c + half - r - step) % row_count) // 2
            pairs.append((r * col_count + c, r * col_count + target))
    return pairs


def right_pairs(row_count, col_count, step):
    pairs = []
    for r in range(row_count):
        for c in range(col_count):
            target = (r - 2 * c - step) % row_count
            pairs.append((r * col_count + c, target * col_count + c))
    return pairs


def body(upper, occupied, tile_molecules):
    row_id = lax.axis_index("row")
    col_id = lax.axis_index("col")
    row_count = lax.axis_size("row")
    col_count = lax.axis_size("col")
    height = upper.shape[0]
    width = upper.shape[1]
    half_width = width // 2
    row_tiles = row_id * TR + jnp.arange(TR, dtype=jnp.int32)
    col_tiles = col_id * (2 * TR) + jnp.arange(2 * TR, dtype=jnp.int32)
    factor = jnp.where(
        row_tiles[:, None] < col_tiles[None, :],
        occupied.astype(jnp.float32),
        jnp.where(row_tiles[:, None] == col_tiles[None, :], 0.5, 0.0),
    )
    half_tri = (upper.reshape(TR, TILE, 2 * TR, TILE) * factor[:, None, :, None]).reshape(
        height, width
    )
    parity = row_id % 2
    halves = half_tri.reshape(height, 2, half_width)
    own_half = jnp.where(parity == 0, halves[:, 0], halves[:, 1]).T
    other_half = jnp.where(parity == 0, halves[:, 1], halves[:, 0]).T
    got_same = send(own_half, mirror_pairs(row_count, col_count, 0))
    got_other = send(other_half, mirror_pairs(row_count, col_count, 1))
    mirrored = jnp.where(
        parity == 0,
        jnp.concatenate([got_same, got_other], axis=1),
        jnp.concatenate([got_other, got_same], axis=1),
    )
    mol_rows = lax.dynamic_slice_in_dim(tile_molecules, row_id * TR, TR)
    mol_cols = lax.dynamic_slice_in_dim(tile_molecules, col_id * (2 * TR), 2 * TR)
    offsets = jnp.arange(TILE, dtype=jnp.int32)
    live_rows = (offsets[None, :] < BASIS * mol_rows[:, None]).astype(jnp.float32).reshape(height)
    live_cols = (offsets[None, :] < BASIS * mol_cols[:, None]).astype(jnp.float32).reshape(width)
    density = (half_tri + mirrored) * live_rows[:, None] * live_cols[None, :]
    group = upper.shape[0]
    col_panel = lax.all_gather(density, "row", axis=0, tiled=True)
    dense_halves = density.reshape(height, 2, half_width)
    pieces = []
    for step in range(2):
        piece = jnp.where((row_id + step) % 2 == 0, dense_halves[:, 0], dense_halves[:, 1])
        pieces.append(send(piece, left_pairs(row_count, col_count, step)))
    left = jnp.concatenate(pieces, axis=1)
    have = 2
    while have < STEPS:
        take = min(have, STEPS - have)
        left = jnp.concatenate([left, shift(left[:, : take * group], "col", have // 2)], axis=1)
        have += take
    start = (row_id + 2 * col_id) % row_count
    doubled = jnp.concatenate([col_panel, col_panel[: STEPS * group]], axis=0)
    right = lax.dynamic_slice_in_dim(doubled, start * group, STEPS * group, axis=0)
    total = jnp.dot(left, right, precision=lax.Precision.HIGHEST, preferred_element_type=jnp.float32)
    return total


def solution(mesh):
    placed = (P("row", "col"), P("row", "col"), P())
    return jax.shard_map(
        body, mesh=mesh, in_specs=placed, out_specs=P("row", "col"), check_vma=False
    )
```

```python
import jax
import jax.numpy as jnp
from jax import lax
from jax.sharding import PartitionSpec as P

BASIS = 23
TILE = 128
TR = 2
STEPS = 14

AXES = ("row", "col")


def send(value, pairs):
    return lax.ppermute(value, AXES, pairs)


def mirror_pairs(row_count, col_count, flip):
    pairs = []
    for r in range(row_count):
        for c in range(col_count):
            half = (r % 2) ^ flip
            target = (2 * c + half, r // 2)
            pairs.append((r * col_count + c, target[0] * col_count + target[1]))
    return pairs


def body(upper, occupied, tile_molecules):
    row_id = lax.axis_index("row")
    col_id = lax.axis_index("col")
    row_count = lax.axis_size("row")
    col_count = lax.axis_size("col")
    height = upper.shape[0]
    width = upper.shape[1]
    half_width = width // 2
    row_tiles = row_id * TR + jnp.arange(TR, dtype=jnp.int32)
    col_tiles = col_id * (2 * TR) + jnp.arange(2 * TR, dtype=jnp.int32)
    factor = jnp.where(
        row_tiles[:, None] < col_tiles[None, :],
        occupied.astype(jnp.float32),
        jnp.where(row_tiles[:, None] == col_tiles[None, :], 0.5, 0.0),
    )
    half_tri = (upper.reshape(TR, TILE, 2 * TR, TILE) * factor[:, None, :, None]).reshape(
        height, width
    )
    parity = row_id % 2
    halves = half_tri.reshape(height, 2, half_width)
    own_half = jnp.where(parity == 0, halves[:, 0], halves[:, 1]).T
    other_half = jnp.where(parity == 0, halves[:, 1], halves[:, 0]).T
    got_same = send(own_half, mirror_pairs(row_count, col_count, 0))
    got_other = send(other_half, mirror_pairs(row_count, col_count, 1))
    mirrored = jnp.where(
        parity == 0,
        jnp.concatenate([got_same, got_other], axis=1),
        jnp.concatenate([got_other, got_same], axis=1),
    )
    mol_rows = lax.dynamic_slice_in_dim(tile_molecules, row_id * TR, TR)
    mol_cols = lax.dynamic_slice_in_dim(tile_molecules, col_id * (2 * TR), 2 * TR)
    offsets = jnp.arange(TILE, dtype=jnp.int32)
    live_rows = (offsets[None, :] < BASIS * mol_rows[:, None]).astype(jnp.float32).reshape(height)
    live_cols = (offsets[None, :] < BASIS * mol_cols[:, None]).astype(jnp.float32).reshape(width)
    density = (half_tri + mirrored) * live_rows[:, None] * live_cols[None, :]
    group = upper.shape[0]
    col_panel = lax.all_gather(density, "row", axis=0, tiled=True)
    start = (row_id + 2 * col_id) % row_count
    picks = (start + jnp.arange(STEPS, dtype=jnp.int32)) % row_count
    right = col_panel.reshape(row_count, group, width)[picks].reshape(STEPS * group, width)
    window = jnp.where(parity == 0, right[:, :half_width], right[:, half_width:])
    left_t = send(window, mirror_pairs(row_count, col_count, 0))
    total = lax.dot_general(
        left_t,
        right,
        (((0,), (0,)), ((), ())),
        precision=lax.Precision.HIGHEST,
        preferred_element_type=jnp.float32,
    )
    return total


def solution(mesh):
    placed = (P("row", "col"), P("row", "col"), P())
    return jax.shard_map(
        body, mesh=mesh, in_specs=placed, out_specs=P("row", "col"), check_vma=False
    )
```

```python
import jax
import jax.numpy as jnp
from jax import lax
from jax.sharding import PartitionSpec as P

BASIS = 23
TILE = 128
TR = 2
STEPS = 14

AXES = ("row", "col")


def send(value, pairs):
    return lax.ppermute(value, AXES, pairs)


def mirror_pairs(row_count, col_count, flip):
    pairs = []
    for r in range(row_count):
        for c in range(col_count):
            half = (r % 2) ^ flip
            target = (2 * c + half, r // 2)
            pairs.append((r * col_count + c, target[0] * col_count + target[1]))
    return pairs


def body(upper, occupied, tile_molecules):
    row_id = lax.axis_index("row")
    col_id = lax.axis_index("col")
    row_count = lax.axis_size("row")
    col_count = lax.axis_size("col")
    height = upper.shape[0]
    width = upper.shape[1]
    half_width = width // 2
    row_tiles = row_id * TR + jnp.arange(TR, dtype=jnp.int32)
    col_tiles = col_id * (2 * TR) + jnp.arange(2 * TR, dtype=jnp.int32)
    factor = jnp.where(
        row_tiles[:, None] < col_tiles[None, :],
        occupied.astype(jnp.float32),
        jnp.where(row_tiles[:, None] == col_tiles[None, :], 0.5, 0.0),
    )
    half_tri = (upper.reshape(TR, TILE, 2 * TR, TILE) * factor[:, None, :, None]).reshape(
        height, width
    )
    parity = row_id % 2
    halves = half_tri.reshape(height, 2, half_width)
    own_half = jnp.where(parity == 0, halves[:, 0], halves[:, 1]).T
    other_half = jnp.where(parity == 0, halves[:, 1], halves[:, 0]).T
    got_same = send(own_half, mirror_pairs(row_count, col_count, 0))
    got_other = send(other_half, mirror_pairs(row_count, col_count, 1))
    mirrored = jnp.where(
        parity == 0,
        jnp.concatenate([got_same, got_other], axis=1),
        jnp.concatenate([got_other, got_same], axis=1),
    )
    mol_rows = lax.dynamic_slice_in_dim(tile_molecules, row_id * TR, TR)
    mol_cols = lax.dynamic_slice_in_dim(tile_molecules, col_id * (2 * TR), 2 * TR)
    offsets = jnp.arange(TILE, dtype=jnp.int32)
    live_rows = (offsets[None, :] < BASIS * mol_rows[:, None]).astype(jnp.float32).reshape(height)
    live_cols = (offsets[None, :] < BASIS * mol_cols[:, None]).astype(jnp.float32).reshape(width)
    density = (half_tri + mirrored) * live_rows[:, None] * live_cols[None, :]
    groups = [list(range(k, col_count, 2)) for k in range(2)]
    own_cols = lax.all_gather(density, "col", axis=0, axis_index_groups=groups)
    mate_cols = lax.ppermute(own_cols, "col", [(i, i ^ 1) for i in range(col_count)])
    pair = jnp.where(col_id % 2 == 0, jnp.stack([own_cols, mate_cols], 1), jnp.stack([mate_cols, own_cols], 1))
    row_panel = jnp.transpose(pair, (2, 0, 1, 3)).reshape(height, col_count * width)
    col_panel = lax.all_gather(density, "row", axis=0, tiled=True)
    group = upper.shape[0]
    total = None
    for step in range(STEPS):
        start = (row_id + 2 * col_id + step) % row_count
        left = lax.dynamic_slice_in_dim(row_panel, start * group, group, axis=1)
        right = lax.dynamic_slice_in_dim(col_panel, start * group, group, axis=0)
        term = jnp.dot(left, right, precision=lax.Precision.HIGHEST, preferred_element_type=jnp.float32)
        total = term if total is None else total + term
    return total


def solution(mesh):
    placed = (P("row", "col"), P("row", "col"), P())
    return jax.shard_map(
        body, mesh=mesh, in_specs=placed, out_specs=P("row", "col"), check_vma=False
    )
```

```python
import jax
import jax.numpy as jnp
from jax import lax
from jax.sharding import PartitionSpec as P

BASIS = 23
TILE = 128
TR = 2
STEPS = 14

AXES = ("row", "col")


def send(value, pairs):
    return lax.ppermute(value, AXES, pairs)


def mirror_pairs(row_count, col_count, flip):
    pairs = []
    for r in range(row_count):
        for c in range(col_count):
            half = (r % 2) ^ flip
            target = (2 * c + half, r // 2)
            pairs.append((r * col_count + c, target[0] * col_count + target[1]))
    return pairs


def body(upper, occupied, tile_molecules):
    row_id = lax.axis_index("row")
    col_id = lax.axis_index("col")
    row_count = lax.axis_size("row")
    col_count = lax.axis_size("col")
    height = upper.shape[0]
    width = upper.shape[1]
    half_width = width // 2
    row_tiles = row_id * TR + jnp.arange(TR, dtype=jnp.int32)
    col_tiles = col_id * (2 * TR) + jnp.arange(2 * TR, dtype=jnp.int32)
    factor = jnp.where(
        row_tiles[:, None] < col_tiles[None, :],
        occupied.astype(jnp.float32),
        jnp.where(row_tiles[:, None] == col_tiles[None, :], 0.5, 0.0),
    )
    half_tri = (upper.reshape(TR, TILE, 2 * TR, TILE) * factor[:, None, :, None]).reshape(
        height, width
    )
    parity = row_id % 2
    halves = half_tri.reshape(height, 2, half_width)
    own_half = jnp.where(parity == 0, halves[:, 0], halves[:, 1]).T
    other_half = jnp.where(parity == 0, halves[:, 1], halves[:, 0]).T
    got_same = send(own_half, mirror_pairs(row_count, col_count, 0))
    got_other = send(other_half, mirror_pairs(row_count, col_count, 1))
    mirrored = jnp.where(
        parity == 0,
        jnp.concatenate([got_same, got_other], axis=1),
        jnp.concatenate([got_other, got_same], axis=1),
    )
    mol_rows = lax.dynamic_slice_in_dim(tile_molecules, row_id * TR, TR)
    mol_cols = lax.dynamic_slice_in_dim(tile_molecules, col_id * (2 * TR), 2 * TR)
    offsets = jnp.arange(TILE, dtype=jnp.int32)
    live_rows = (offsets[None, :] < BASIS * mol_rows[:, None]).astype(jnp.float32).reshape(height)
    live_cols = (offsets[None, :] < BASIS * mol_cols[:, None]).astype(jnp.float32).reshape(width)
    density = (half_tri + mirrored) * live_rows[:, None] * live_cols[None, :]
    groups = [list(range(k, col_count, 2)) for k in range(2)]
    own_cols = lax.all_gather(density, "col", axis=0, axis_index_groups=groups)
    mate_cols = lax.ppermute(own_cols, "col", [(i, i ^ 1) for i in range(col_count)])
    pair = jnp.where(col_id % 2 == 0, jnp.stack([own_cols, mate_cols], 1), jnp.stack([mate_cols, own_cols], 1))
    row_panel = jnp.transpose(pair, (2, 0, 1, 3)).reshape(height, col_count * width)
    col_panel = lax.all_gather(density, "row", axis=0, tiled=True)
    group = upper.shape[0]
    start = (row_id + 2 * col_id) % row_count
    picks = (start + jnp.arange(STEPS, dtype=jnp.int32)) % row_count
    left = row_panel.reshape(height, row_count, group)[:, picks].reshape(height, STEPS * group)
    right = col_panel.reshape(row_count, group, width)[picks].reshape(STEPS * group, width)
    total = jnp.dot(left, right, precision=lax.Precision.HIGHEST, preferred_element_type=jnp.float32)
    return total


def solution(mesh):
    placed = (P("row", "col"), P("row", "col"), P())
    return jax.shard_map(
        body, mesh=mesh, in_specs=placed, out_specs=P("row", "col"), check_vma=False
    )
```

```python
import jax
import jax.numpy as jnp
from jax import lax
from jax.sharding import PartitionSpec as P

BASIS = 23
TILE = 128
TR = 2
STEPS = 14

AXES = ("row", "col")


def send(value, pairs):
    return lax.ppermute(value, AXES, pairs)


def mirror_pairs(row_count, col_count, flip):
    pairs = []
    for r in range(row_count):
        for c in range(col_count):
            half = (r % 2) ^ flip
            target = (2 * c + half, r // 2)
            pairs.append((r * col_count + c, target[0] * col_count + target[1]))
    return pairs


def shift(value, axis, by):
    length = lax.axis_size(axis)
    return lax.ppermute(value, axis, [(i, (i - by) % length) for i in range(length)])


def left_pairs(row_count, col_count, step):
    pairs = []
    for r in range(row_count):
        half = (r + step) % 2
        for c in range(col_count):
            target = ((2 * c + half - r - step) % row_count) // 2
            pairs.append((r * col_count + c, r * col_count + target))
    return pairs


def body(upper, occupied, tile_molecules):
    row_id = lax.axis_index("row")
    col_id = lax.axis_index("col")
    row_count = lax.axis_size("row")
    col_count = lax.axis_size("col")
    height = upper.shape[0]
    width = upper.shape[1]
    half_width = width // 2
    row_tiles = row_id * TR + jnp.arange(TR, dtype=jnp.int32)
    col_tiles = col_id * (2 * TR) + jnp.arange(2 * TR, dtype=jnp.int32)
    factor = jnp.where(
        row_tiles[:, None] < col_tiles[None, :],
        occupied.astype(jnp.float32),
        jnp.where(row_tiles[:, None] == col_tiles[None, :], 0.5, 0.0),
    )
    half_tri = (upper.reshape(TR, TILE, 2 * TR, TILE) * factor[:, None, :, None]).reshape(
        height, width
    )
    parity = row_id % 2
    halves = half_tri.reshape(height, 2, half_width)
    own_half = jnp.where(parity == 0, halves[:, 0], halves[:, 1]).T
    other_half = jnp.where(parity == 0, halves[:, 1], halves[:, 0]).T
    got_same = send(own_half, mirror_pairs(row_count, col_count, 0))
    got_other = send(other_half, mirror_pairs(row_count, col_count, 1))
    mirrored = jnp.where(
        parity == 0,
        jnp.concatenate([got_same, got_other], axis=1),
        jnp.concatenate([got_other, got_same], axis=1),
    )
    mol_rows = lax.dynamic_slice_in_dim(tile_molecules, row_id * TR, TR)
    mol_cols = lax.dynamic_slice_in_dim(tile_molecules, col_id * (2 * TR), 2 * TR)
    offsets = jnp.arange(TILE, dtype=jnp.int32)
    live_rows = (offsets[None, :] < BASIS * mol_rows[:, None]).astype(jnp.float32).reshape(height)
    live_cols = (offsets[None, :] < BASIS * mol_cols[:, None]).astype(jnp.float32).reshape(width)
    density = (half_tri + mirrored) * live_rows[:, None] * live_cols[None, :]
    dense_halves = density.reshape(height, 2, half_width)
    parts = []
    for step in range(2):
        piece = jnp.where((row_id + step) % 2 == 0, dense_halves[:, 0], dense_halves[:, 1])
        parts.append(send(piece, left_pairs(row_count, col_count, step)))
    window = jnp.concatenate(parts, axis=1)
    for _ in range(STEPS // 2 - 1):
        window = shift(window, "col", 1)
        parts.append(window)
    left = jnp.concatenate(parts, axis=1)
    col_panel = lax.all_gather(density, "row", axis=0, tiled=True)
    group = upper.shape[0]
    start = (row_id + 2 * col_id) % row_count
    picks = (start + jnp.arange(STEPS, dtype=jnp.int32)) % row_count
    right = col_panel.reshape(row_count, group, width)[picks].reshape(STEPS * group, width)
    total = jnp.dot(left, right, precision=lax.Precision.HIGHEST, preferred_element_type=jnp.float32)
    return total


def solution(mesh):
    placed = (P("row", "col"), P("row", "col"), P())
    return jax.shard_map(
        body, mesh=mesh, in_specs=placed, out_specs=P("row", "col"), check_vma=False
    )
```

```python
import jax
import jax.numpy as jnp
from jax import lax
from jax.sharding import PartitionSpec as P

BASIS = 23
TILE = 128
TR = 2
STEPS = 14

AXES = ("row", "col")


def send(value, pairs):
    return lax.ppermute(value, AXES, pairs)


def mirror_pairs(row_count, col_count, flip):
    pairs = []
    for r in range(row_count):
        for c in range(col_count):
            half = (r % 2) ^ flip
            target = (2 * c + half, r // 2)
            pairs.append((r * col_count + c, target[0] * col_count + target[1]))
    return pairs


def shift(value, axis, by):
    length = lax.axis_size(axis)
    return lax.ppermute(value, axis, [(i, (i - by) % length) for i in range(length)])


def left_pairs(row_count, col_count, step):
    pairs = []
    for r in range(row_count):
        half = (r + step) % 2
        for c in range(col_count):
            target = ((2 * c + half - r - step) % row_count) // 2
            pairs.append((r * col_count + c, r * col_count + target))
    return pairs


def body(upper, occupied, tile_molecules):
    row_id = lax.axis_index("row")
    col_id = lax.axis_index("col")
    row_count = lax.axis_size("row")
    col_count = lax.axis_size("col")
    height = upper.shape[0]
    width = upper.shape[1]
    half_width = width // 2
    row_tiles = row_id * TR + jnp.arange(TR, dtype=jnp.int32)
    col_tiles = col_id * (2 * TR) + jnp.arange(2 * TR, dtype=jnp.int32)
    factor = jnp.where(
        row_tiles[:, None] < col_tiles[None, :],
        occupied.astype(jnp.float32),
        jnp.where(row_tiles[:, None] == col_tiles[None, :], 0.5, 0.0),
    )
    half_tri = (upper.reshape(TR, TILE, 2 * TR, TILE) * factor[:, None, :, None]).reshape(
        height, width
    )
    parity = row_id % 2
    halves = half_tri.reshape(height, 2, half_width)
    own_half = jnp.where(parity == 0, halves[:, 0], halves[:, 1]).T
    other_half = jnp.where(parity == 0, halves[:, 1], halves[:, 0]).T
    got_same = send(own_half, mirror_pairs(row_count, col_count, 0))
    got_other = send(other_half, mirror_pairs(row_count, col_count, 1))
    mirrored = jnp.where(
        parity == 0,
        jnp.concatenate([got_same, got_other], axis=1),
        jnp.concatenate([got_other, got_same], axis=1),
    )
    mol_rows = lax.dynamic_slice_in_dim(tile_molecules, row_id * TR, TR)
    mol_cols = lax.dynamic_slice_in_dim(tile_molecules, col_id * (2 * TR), 2 * TR)
    offsets = jnp.arange(TILE, dtype=jnp.int32)
    live_rows = (offsets[None, :] < BASIS * mol_rows[:, None]).astype(jnp.float32).reshape(height)
    live_cols = (offsets[None, :] < BASIS * mol_cols[:, None]).astype(jnp.float32).reshape(width)
    density = (half_tri + mirrored) * live_rows[:, None] * live_cols[None, :]
    dense_halves = density.reshape(height, 2, half_width)
    middle = STEPS // 2 - 1
    parts = []
    for step in (middle, middle + 1):
        piece = jnp.where((row_id + step) % 2 == 0, dense_halves[:, 0], dense_halves[:, 1])
        parts.append(send(piece, left_pairs(row_count, col_count, step)))
    centre = jnp.concatenate(parts, axis=1)
    ahead = centre
    behind = centre
    after = []
    before = []
    for _ in range(middle // 2):
        ahead = shift(ahead, "col", 1)
        behind = shift(behind, "col", -1)
        after.append(ahead)
        before.insert(0, behind)
    parts = before + [centre] + after
    left = jnp.concatenate(parts, axis=1)
    col_panel = lax.all_gather(density, "row", axis=0, tiled=True)
    group = upper.shape[0]
    start = (row_id + 2 * col_id) % row_count
    picks = (start + jnp.arange(STEPS, dtype=jnp.int32)) % row_count
    right = col_panel.reshape(row_count, group, width)[picks].reshape(STEPS * group, width)
    total = jnp.dot(left, right, precision=lax.Precision.HIGHEST, preferred_element_type=jnp.float32)
    return total


def solution(mesh):
    placed = (P("row", "col"), P("row", "col"), P())
    return jax.shard_map(
        body, mesh=mesh, in_specs=placed, out_specs=P("row", "col"), check_vma=False
    )
```

```python
import jax
import jax.numpy as jnp
from jax import lax
from jax.sharding import PartitionSpec as P

BASIS = 23
TILE = 128
TR = 2
STEPS = 14

AXES = ("row", "col")


def send(value, pairs):
    return lax.ppermute(value, AXES, pairs)


def mirror_pairs(row_count, col_count, flip):
    pairs = []
    for r in range(row_count):
        for c in range(col_count):
            half = (r % 2) ^ flip
            target = (2 * c + half, r // 2)
            pairs.append((r * col_count + c, target[0] * col_count + target[1]))
    return pairs


def shift(value, axis, by):
    length = lax.axis_size(axis)
    return lax.ppermute(value, axis, [(i, (i - by) % length) for i in range(length)])


def left_pairs(row_count, col_count, step):
    pairs = []
    for r in range(row_count):
        half = (r + step) % 2
        for c in range(col_count):
            target = ((2 * c + half - r - step) % row_count) // 2
            pairs.append((r * col_count + c, r * col_count + target))
    return pairs


def right_pairs(row_count, col_count, step):
    pairs = []
    for r in range(row_count):
        for c in range(col_count):
            target = (r - 2 * c - step) % row_count
            pairs.append((r * col_count + c, target * col_count + c))
    return pairs


def body(upper, occupied, tile_molecules):
    row_id = lax.axis_index("row")
    col_id = lax.axis_index("col")
    row_count = lax.axis_size("row")
    col_count = lax.axis_size("col")
    height = upper.shape[0]
    width = upper.shape[1]
    half_width = width // 2
    row_tiles = row_id * TR + jnp.arange(TR, dtype=jnp.int32)
    col_tiles = col_id * (2 * TR) + jnp.arange(2 * TR, dtype=jnp.int32)
    factor = jnp.where(
        row_tiles[:, None] < col_tiles[None, :],
        occupied.astype(jnp.float32),
        jnp.where(row_tiles[:, None] == col_tiles[None, :], 0.5, 0.0),
    )
    half_tri = (upper.reshape(TR, TILE, 2 * TR, TILE) * factor[:, None, :, None]).reshape(
        height, width
    )
    parity = row_id % 2
    halves = half_tri.reshape(height, 2, half_width)
    own_half = jnp.where(parity == 0, halves[:, 0], halves[:, 1]).T
    other_half = jnp.where(parity == 0, halves[:, 1], halves[:, 0]).T
    got_same = send(own_half, mirror_pairs(row_count, col_count, 0))
    got_other = send(other_half, mirror_pairs(row_count, col_count, 1))
    mirrored = jnp.where(
        parity == 0,
        jnp.concatenate([got_same, got_other], axis=1),
        jnp.concatenate([got_other, got_same], axis=1),
    )
    mol_rows = lax.dynamic_slice_in_dim(tile_molecules, row_id * TR, TR)
    mol_cols = lax.dynamic_slice_in_dim(tile_molecules, col_id * (2 * TR), 2 * TR)
    offsets = jnp.arange(TILE, dtype=jnp.int32)
    live_rows = (offsets[None, :] < BASIS * mol_rows[:, None]).astype(jnp.float32).reshape(height)
    live_cols = (offsets[None, :] < BASIS * mol_cols[:, None]).astype(jnp.float32).reshape(width)
    density = (half_tri + mirrored) * live_rows[:, None] * live_cols[None, :]
    group = upper.shape[0]
    row_panel = lax.all_gather(density, "col", axis=1, tiled=True)
    middle = STEPS // 2 - 1
    centre = send(density, right_pairs(row_count, col_count, middle))
    ahead = centre
    behind = centre
    after = []
    before = []
    for _ in range(STEPS - 1 - middle):
        ahead = shift(ahead, "row", 1)
        after.append(ahead)
    for _ in range(middle):
        behind = shift(behind, "row", -1)
        before.insert(0, behind)
    right = jnp.concatenate(before + [centre] + after, axis=0)
    start = (row_id + 2 * col_id) % row_count
    picks = (start + jnp.arange(STEPS, dtype=jnp.int32)) % row_count
    left = row_panel.reshape(height, row_count, group)[:, picks].reshape(height, STEPS * group)
    total = jnp.dot(left, right, precision=lax.Precision.HIGHEST, preferred_element_type=jnp.float32)
    return total


def solution(mesh):
    placed = (P("row", "col"), P("row", "col"), P())
    return jax.shard_map(
        body, mesh=mesh, in_specs=placed, out_specs=P("row", "col"), check_vma=False
    )
```

```python
import jax
import jax.numpy as jnp
from jax import lax
from jax.sharding import PartitionSpec as P

BASIS = 23
TILE = 128
TR = 2
STEPS = 14

AXES = ("row", "col")


def send(value, pairs):
    return lax.ppermute(value, AXES, pairs)


def mirror_pairs(row_count, col_count, flip):
    pairs = []
    for r in range(row_count):
        for c in range(col_count):
            half = (r % 2) ^ flip
            target = (2 * c + half, r // 2)
            pairs.append((r * col_count + c, target[0] * col_count + target[1]))
    return pairs


def shift(value, axis, by):
    length = lax.axis_size(axis)
    return lax.ppermute(value, axis, [(i, (i - by) % length) for i in range(length)])


def left_pairs(row_count, col_count, step):
    pairs = []
    for r in range(row_count):
        half = (r + step) % 2
        for c in range(col_count):
            target = ((2 * c + half - r - step) % row_count) // 2
            pairs.append((r * col_count + c, r * col_count + target))
    return pairs


def right_pairs(row_count, col_count, step):
    pairs = []
    for r in range(row_count):
        for c in range(col_count):
            target = (r - 2 * c - step) % row_count
            pairs.append((r * col_count + c, target * col_count + c))
    return pairs


def body(upper, occupied, tile_molecules):
    row_id = lax.axis_index("row")
    col_id = lax.axis_index("col")
    row_count = lax.axis_size("row")
    col_count = lax.axis_size("col")
    height = upper.shape[0]
    width = upper.shape[1]
    half_width = width // 2
    row_tiles = row_id * TR + jnp.arange(TR, dtype=jnp.int32)
    col_tiles = col_id * (2 * TR) + jnp.arange(2 * TR, dtype=jnp.int32)
    factor = jnp.where(
        row_tiles[:, None] < col_tiles[None, :],
        occupied.astype(jnp.float32),
        jnp.where(row_tiles[:, None] == col_tiles[None, :], 0.5, 0.0),
    )
    half_tri = (upper.reshape(TR, TILE, 2 * TR, TILE) * factor[:, None, :, None]).reshape(
        height, width
    )
    parity = row_id % 2
    halves = half_tri.reshape(height, 2, half_width)
    own_half = jnp.where(parity == 0, halves[:, 0], halves[:, 1]).T
    other_half = jnp.where(parity == 0, halves[:, 1], halves[:, 0]).T
    got_same = send(own_half, mirror_pairs(row_count, col_count, 0))
    got_other = send(other_half, mirror_pairs(row_count, col_count, 1))
    mirrored = jnp.where(
        parity == 0,
        jnp.concatenate([got_same, got_other], axis=1),
        jnp.concatenate([got_other, got_same], axis=1),
    )
    mol_rows = lax.dynamic_slice_in_dim(tile_molecules, row_id * TR, TR)
    mol_cols = lax.dynamic_slice_in_dim(tile_molecules, col_id * (2 * TR), 2 * TR)
    offsets = jnp.arange(TILE, dtype=jnp.int32)
    live_rows = (offsets[None, :] < BASIS * mol_rows[:, None]).astype(jnp.float32).reshape(height)
    live_cols = (offsets[None, :] < BASIS * mol_cols[:, None]).astype(jnp.float32).reshape(width)
    density = (half_tri + mirrored) * live_rows[:, None] * live_cols[None, :]
    group = upper.shape[0]
    row_panel = lax.all_gather(density, "col", axis=1, tiled=True)
    middle = STEPS // 2 - 1
    centre = send(density, right_pairs(row_count, col_count, middle))
    ahead = centre
    behind = centre
    after = []
    before = []
    for _ in range(STEPS - 1 - middle):
        ahead = shift(ahead, "row", 1)
        after.append(ahead)
    for _ in range(middle):
        behind = shift(behind, "row", -1)
        before.insert(0, behind)
    pieces = before + [centre] + after
    total = None
    for step in range(STEPS):
        start = (row_id + 2 * col_id + step) % row_count
        left = lax.dynamic_slice_in_dim(row_panel, start * group, group, axis=1)
        term = jnp.dot(left, pieces[step], precision=lax.Precision.HIGHEST, preferred_element_type=jnp.float32)
        total = term if total is None else total + term
    return total


def solution(mesh):
    placed = (P("row", "col"), P("row", "col"), P())
    return jax.shard_map(
        body, mesh=mesh, in_specs=placed, out_specs=P("row", "col"), check_vma=False
    )
```

```python
import jax
import jax.numpy as jnp
from jax import lax
from jax.sharding import PartitionSpec as P

BASIS = 23
TILE = 128
TR = 2
STEPS = 14

AXES = ("row", "col")


def send(value, pairs):
    return lax.ppermute(value, AXES, pairs)


def mirror_pairs(row_count, col_count, flip):
    pairs = []
    for r in range(row_count):
        for c in range(col_count):
            half = (r % 2) ^ flip
            target = (2 * c + half, r // 2)
            pairs.append((r * col_count + c, target[0] * col_count + target[1]))
    return pairs


def shift(value, axis, by):
    length = lax.axis_size(axis)
    return lax.ppermute(value, axis, [(i, (i - by) % length) for i in range(length)])


def left_pairs(row_count, col_count, step):
    pairs = []
    for r in range(row_count):
        half = (r + step) % 2
        for c in range(col_count):
            target = ((2 * c + half - r - step) % row_count) // 2
            pairs.append((r * col_count + c, r * col_count + target))
    return pairs


def right_pairs(row_count, col_count, step):
    pairs = []
    for r in range(row_count):
        for c in range(col_count):
            target = (r - 2 * c - step) % row_count
            pairs.append((r * col_count + c, target * col_count + c))
    return pairs


def body(upper, occupied, tile_molecules):
    row_id = lax.axis_index("row")
    col_id = lax.axis_index("col")
    row_count = lax.axis_size("row")
    col_count = lax.axis_size("col")
    height = upper.shape[0]
    width = upper.shape[1]
    half_width = width // 2
    row_tiles = row_id * TR + jnp.arange(TR, dtype=jnp.int32)
    col_tiles = col_id * (2 * TR) + jnp.arange(2 * TR, dtype=jnp.int32)
    factor = jnp.where(
        row_tiles[:, None] < col_tiles[None, :],
        occupied.astype(jnp.float32),
        jnp.where(row_tiles[:, None] == col_tiles[None, :], 0.5, 0.0),
    )
    half_tri = (upper.reshape(TR, TILE, 2 * TR, TILE) * factor[:, None, :, None]).reshape(
        height, width
    )
    parity = row_id % 2
    halves = half_tri.reshape(height, 2, half_width)
    own_half = jnp.where(parity == 0, halves[:, 0], halves[:, 1]).T
    other_half = jnp.where(parity == 0, halves[:, 1], halves[:, 0]).T
    got_same = send(own_half, mirror_pairs(row_count, col_count, 0))
    got_other = send(other_half, mirror_pairs(row_count, col_count, 1))
    mirrored = jnp.where(
        parity == 0,
        jnp.concatenate([got_same, got_other], axis=1),
        jnp.concatenate([got_other, got_same], axis=1),
    )
    mol_rows = lax.dynamic_slice_in_dim(tile_molecules, row_id * TR, TR)
    mol_cols = lax.dynamic_slice_in_dim(tile_molecules, col_id * (2 * TR), 2 * TR)
    offsets = jnp.arange(TILE, dtype=jnp.int32)
    live_rows = (offsets[None, :] < BASIS * mol_rows[:, None]).astype(jnp.float32).reshape(height)
    live_cols = (offsets[None, :] < BASIS * mol_cols[:, None]).astype(jnp.float32).reshape(width)
    density = (half_tri + mirrored) * live_rows[:, None] * live_cols[None, :]
    group = upper.shape[0]
    row_panel = lax.all_gather(density, "col", axis=1, tiled=True)
    middle = STEPS // 2 - 1
    centre = send(density, right_pairs(row_count, col_count, middle))
    ahead = centre
    behind = centre
    after = []
    before = []
    for _ in range(STEPS - 1 - middle):
        ahead = shift(ahead, "row", 1)
        after.append(ahead)
    for _ in range(middle):
        behind = shift(behind, "row", -1)
        before.insert(0, behind)
    pieces = before + [centre] + after
    total = None
    for step in range(0, STEPS, 2):
        lefts = []
        for offset in range(2):
            start = (row_id + 2 * col_id + step + offset) % row_count
            lefts.append(lax.dynamic_slice_in_dim(row_panel, start * group, group, axis=1))
        left = jnp.concatenate(lefts, axis=1)
        right = jnp.concatenate(pieces[step : step + 2], axis=0)
        term = jnp.dot(left, right, precision=lax.Precision.HIGHEST, preferred_element_type=jnp.float32)
        total = term if total is None else total + term
    return total


def solution(mesh):
    placed = (P("row", "col"), P("row", "col"), P())
    return jax.shard_map(
        body, mesh=mesh, in_specs=placed, out_specs=P("row", "col"), check_vma=False
    )
```

```python
import jax
import jax.numpy as jnp
from jax import lax
from jax.sharding import PartitionSpec as P

BASIS = 23
TILE = 128
TR = 2
STEPS = 14

AXES = ("row", "col")


def send(value, pairs):
    return lax.ppermute(value, AXES, pairs)


def mirror_pairs(row_count, col_count, flip):
    pairs = []
    for r in range(row_count):
        for c in range(col_count):
            half = (r % 2) ^ flip
            target = (2 * c + half, r // 2)
            pairs.append((r * col_count + c, target[0] * col_count + target[1]))
    return pairs


def shift(value, axis, by):
    length = lax.axis_size(axis)
    return lax.ppermute(value, axis, [(i, (i - by) % length) for i in range(length)])


def left_pairs(row_count, col_count, step):
    pairs = []
    for r in range(row_count):
        half = (r + step) % 2
        for c in range(col_count):
            target = ((2 * c + half - r - step) % row_count) // 2
            pairs.append((r * col_count + c, r * col_count + target))
    return pairs


def right_pairs(row_count, col_count, step):
    pairs = []
    for r in range(row_count):
        for c in range(col_count):
            target = (r - 2 * c - step) % row_count
            pairs.append((r * col_count + c, target * col_count + c))
    return pairs


def body(upper, occupied, tile_molecules):
    row_id = lax.axis_index("row")
    col_id = lax.axis_index("col")
    row_count = lax.axis_size("row")
    col_count = lax.axis_size("col")
    height = upper.shape[0]
    width = upper.shape[1]
    half_width = width // 2
    row_tiles = row_id * TR + jnp.arange(TR, dtype=jnp.int32)
    col_tiles = col_id * (2 * TR) + jnp.arange(2 * TR, dtype=jnp.int32)
    factor = jnp.where(
        row_tiles[:, None] < col_tiles[None, :],
        occupied.astype(jnp.float32),
        jnp.where(row_tiles[:, None] == col_tiles[None, :], 0.5, 0.0),
    )
    half_tri = (upper.reshape(TR, TILE, 2 * TR, TILE) * factor[:, None, :, None]).reshape(
        height, width
    )
    parity = row_id % 2
    halves = half_tri.reshape(height, 2, half_width)
    own_half = jnp.where(parity == 0, halves[:, 0], halves[:, 1]).T
    other_half = jnp.where(parity == 0, halves[:, 1], halves[:, 0]).T
    got_same = send(own_half, mirror_pairs(row_count, col_count, 0))
    got_other = send(other_half, mirror_pairs(row_count, col_count, 1))
    mirrored = jnp.where(
        parity == 0,
        jnp.concatenate([got_same, got_other], axis=1),
        jnp.concatenate([got_other, got_same], axis=1),
    )
    mol_rows = lax.dynamic_slice_in_dim(tile_molecules, row_id * TR, TR)
    mol_cols = lax.dynamic_slice_in_dim(tile_molecules, col_id * (2 * TR), 2 * TR)
    offsets = jnp.arange(TILE, dtype=jnp.int32)
    live_rows = (offsets[None, :] < BASIS * mol_rows[:, None]).astype(jnp.float32).reshape(height)
    live_cols = (offsets[None, :] < BASIS * mol_cols[:, None]).astype(jnp.float32).reshape(width)
    density = (half_tri + mirrored) * live_rows[:, None] * live_cols[None, :]
    group = upper.shape[0]
    row_panel = lax.all_gather(density, "col", axis=1, tiled=True)
    middle = STEPS // 2
    centre = send(density, right_pairs(row_count, col_count, middle))
    ahead = centre
    behind = centre
    after = []
    before = []
    for _ in range(STEPS - 1 - middle):
        ahead = shift(ahead, "row", 1)
        after.append(ahead)
    for _ in range(middle):
        behind = shift(behind, "row", -1)
        before.insert(0, behind)
    pieces = before + [centre] + after
    total = None
    for step in range(0, STEPS, 2):
        lefts = []
        for offset in range(2):
            start = (row_id + 2 * col_id + step + offset) % row_count
            lefts.append(lax.dynamic_slice_in_dim(row_panel, start * group, group, axis=1))
        left = jnp.concatenate(lefts, axis=1)
        right = jnp.concatenate(pieces[step : step + 2], axis=0)
        term = jnp.dot(left, right, precision=lax.Precision.HIGHEST, preferred_element_type=jnp.float32)
        total = term if total is None else total + term
    return total


def solution(mesh):
    placed = (P("row", "col"), P("row", "col"), P())
    return jax.shard_map(
        body, mesh=mesh, in_specs=placed, out_specs=P("row", "col"), check_vma=False
    )
```

```python
import jax
import jax.numpy as jnp
from jax import lax
from jax.sharding import PartitionSpec as P

BASIS = 23
TILE = 128
TR = 2
STEPS = 14

AXES = ("row", "col")


def send(value, pairs):
    return lax.ppermute(value, AXES, pairs)


def mirror_pairs(row_count, col_count, flip):
    pairs = []
    for r in range(row_count):
        for c in range(col_count):
            half = (r % 2) ^ flip
            target = (2 * c + half, r // 2)
            pairs.append((r * col_count + c, target[0] * col_count + target[1]))
    return pairs


def shift(value, axis, by):
    length = lax.axis_size(axis)
    return lax.ppermute(value, axis, [(i, (i - by) % length) for i in range(length)])


def left_pairs(row_count, col_count, step):
    pairs = []
    for r in range(row_count):
        half = (r + step) % 2
        for c in range(col_count):
            target = ((2 * c + half - r - step) % row_count) // 2
            pairs.append((r * col_count + c, r * col_count + target))
    return pairs


def right_pairs(row_count, col_count, step):
    pairs = []
    for r in range(row_count):
        for c in range(col_count):
            target = (r - 2 * c - step) % row_count
            pairs.append((r * col_count + c, target * col_count + c))
    return pairs


def body(upper, occupied, tile_molecules):
    row_id = lax.axis_index("row")
    col_id = lax.axis_index("col")
    row_count = lax.axis_size("row")
    col_count = lax.axis_size("col")
    height = upper.shape[0]
    width = upper.shape[1]
    half_width = width // 2
    row_tiles = row_id * TR + jnp.arange(TR, dtype=jnp.int32)
    col_tiles = col_id * (2 * TR) + jnp.arange(2 * TR, dtype=jnp.int32)
    factor = jnp.where(
        row_tiles[:, None] < col_tiles[None, :],
        occupied.astype(jnp.float32),
        jnp.where(row_tiles[:, None] == col_tiles[None, :], 0.5, 0.0),
    )
    half_tri = (upper.reshape(TR, TILE, 2 * TR, TILE) * factor[:, None, :, None]).reshape(
        height, width
    )
    parity = row_id % 2
    halves = half_tri.reshape(height, 2, half_width)
    own_half = jnp.where(parity == 0, halves[:, 0], halves[:, 1]).T
    other_half = jnp.where(parity == 0, halves[:, 1], halves[:, 0]).T
    got_same = send(own_half, mirror_pairs(row_count, col_count, 0))
    got_other = send(other_half, mirror_pairs(row_count, col_count, 1))
    mirrored = jnp.where(
        parity == 0,
        jnp.concatenate([got_same, got_other], axis=1),
        jnp.concatenate([got_other, got_same], axis=1),
    )
    mol_rows = lax.dynamic_slice_in_dim(tile_molecules, row_id * TR, TR)
    mol_cols = lax.dynamic_slice_in_dim(tile_molecules, col_id * (2 * TR), 2 * TR)
    offsets = jnp.arange(TILE, dtype=jnp.int32)
    live_rows = (offsets[None, :] < BASIS * mol_rows[:, None]).astype(jnp.float32).reshape(height)
    live_cols = (offsets[None, :] < BASIS * mol_cols[:, None]).astype(jnp.float32).reshape(width)
    density = (half_tri + mirrored) * live_rows[:, None] * live_cols[None, :]
    group = upper.shape[0]
    row_panel = lax.all_gather(density, "col", axis=1, tiled=True)
    split = STEPS // 2
    spans = ((3, split - 1 - 3), (4, STEPS - split - 1 - 4))
    centres = [send(density, right_pairs(row_count, col_count, split * k + back)) for k, (back, _) in enumerate(spans)]
    lanes = [([], [centre], []) for centre in centres]
    for direction, side in ((1, 2), (-1, 0)):
        states = list(centres)
        for step in range(max(spans[k][0 if direction < 0 else 1] for k in range(2))):
            live = [k for k in range(2) if step < spans[k][0 if direction < 0 else 1]]
            moved = shift(jnp.stack([states[k] for k in live]), "row", direction)
            for slot, k in enumerate(live):
                states[k] = moved[slot]
                if direction > 0:
                    lanes[k][side].append(moved[slot])
                else:
                    lanes[k][side].insert(0, moved[slot])
    pieces = [p for lane in lanes for part in lane for p in part]
    total = None
    for step in range(0, STEPS, 2):
        lefts = []
        for offset in range(2):
            start = (row_id + 2 * col_id + step + offset) % row_count
            lefts.append(lax.dynamic_slice_in_dim(row_panel, start * group, group, axis=1))
        left = jnp.concatenate(lefts, axis=1)
        right = jnp.concatenate(pieces[step : step + 2], axis=0)
        term = jnp.dot(left, right, precision=lax.Precision.HIGHEST, preferred_element_type=jnp.float32)
        total = term if total is None else total + term
    return total


def solution(mesh):
    placed = (P("row", "col"), P("row", "col"), P())
    return jax.shard_map(
        body, mesh=mesh, in_specs=placed, out_specs=P("row", "col"), check_vma=False
    )
```

```python
import jax
import jax.numpy as jnp
from jax import lax
from jax.sharding import PartitionSpec as P

BASIS = 23
TILE = 128
TR = 2
STEPS = 14

AXES = ("row", "col")


def send(value, pairs):
    return lax.ppermute(value, AXES, pairs)


def mirror_pairs(row_count, col_count, flip):
    pairs = []
    for r in range(row_count):
        for c in range(col_count):
            half = (r % 2) ^ flip
            target = (2 * c + half, r // 2)
            pairs.append((r * col_count + c, target[0] * col_count + target[1]))
    return pairs


def shift(value, axis, by):
    length = lax.axis_size(axis)
    return lax.ppermute(value, axis, [(i, (i - by) % length) for i in range(length)])


def left_pairs(row_count, col_count, step):
    pairs = []
    for r in range(row_count):
        half = (r + step) % 2
        for c in range(col_count):
            target = ((2 * c + half - r - step) % row_count) // 2
            pairs.append((r * col_count + c, r * col_count + target))
    return pairs


def right_pairs(row_count, col_count, step):
    pairs = []
    for r in range(row_count):
        for c in range(col_count):
            target = (r - 2 * c - step) % row_count
            pairs.append((r * col_count + c, target * col_count + c))
    return pairs


def body(upper, occupied, tile_molecules):
    row_id = lax.axis_index("row")
    col_id = lax.axis_index("col")
    row_count = lax.axis_size("row")
    col_count = lax.axis_size("col")
    height = upper.shape[0]
    width = upper.shape[1]
    half_width = width // 2
    row_tiles = row_id * TR + jnp.arange(TR, dtype=jnp.int32)
    col_tiles = col_id * (2 * TR) + jnp.arange(2 * TR, dtype=jnp.int32)
    factor = jnp.where(
        row_tiles[:, None] < col_tiles[None, :],
        occupied.astype(jnp.float32),
        jnp.where(row_tiles[:, None] == col_tiles[None, :], 0.5, 0.0),
    )
    half_tri = (upper.reshape(TR, TILE, 2 * TR, TILE) * factor[:, None, :, None]).reshape(
        height, width
    )
    parity = row_id % 2
    halves = half_tri.reshape(height, 2, half_width)
    own_half = jnp.where(parity == 0, halves[:, 0], halves[:, 1]).T
    other_half = jnp.where(parity == 0, halves[:, 1], halves[:, 0]).T
    got_same = send(own_half, mirror_pairs(row_count, col_count, 0))
    got_other = send(other_half, mirror_pairs(row_count, col_count, 1))
    mirrored = jnp.where(
        parity == 0,
        jnp.concatenate([got_same, got_other], axis=1),
        jnp.concatenate([got_other, got_same], axis=1),
    )
    mol_rows = lax.dynamic_slice_in_dim(tile_molecules, row_id * TR, TR)
    mol_cols = lax.dynamic_slice_in_dim(tile_molecules, col_id * (2 * TR), 2 * TR)
    offsets = jnp.arange(TILE, dtype=jnp.int32)
    live_rows = (offsets[None, :] < BASIS * mol_rows[:, None]).astype(jnp.float32).reshape(height)
    live_cols = (offsets[None, :] < BASIS * mol_cols[:, None]).astype(jnp.float32).reshape(width)
    density = (half_tri + mirrored) * live_rows[:, None] * live_cols[None, :]
    group = upper.shape[0]
    row_panel = lax.all_gather(density, "col", axis=1, tiled=True)
    middle = STEPS // 2
    centre = send(density, right_pairs(row_count, col_count, middle))
    first_ahead = shift(centre, "row", 1)
    first_behind = shift(centre, "row", -1)
    ahead = jnp.stack([centre, first_ahead])
    behind = jnp.stack([first_behind, centre])
    after = [first_ahead]
    before = [first_behind]
    for _ in range(2):
        ahead = shift(ahead, "row", 2)
        after += [ahead[0], ahead[1]]
    for _ in range(3):
        behind = shift(behind, "row", -2)
        before = [behind[0], behind[1]] + before
    after.append(shift(ahead[0], "row", 2))
    pieces = before + [centre] + after
    total = None
    for step in range(0, STEPS, 2):
        lefts = []
        for offset in range(2):
            start = (row_id + 2 * col_id + step + offset) % row_count
            lefts.append(lax.dynamic_slice_in_dim(row_panel, start * group, group, axis=1))
        left = jnp.concatenate(lefts, axis=1)
        right = jnp.concatenate(pieces[step : step + 2], axis=0)
        term = jnp.dot(left, right, precision=lax.Precision.HIGHEST, preferred_element_type=jnp.float32)
        total = term if total is None else total + term
    return total


def solution(mesh):
    placed = (P("row", "col"), P("row", "col"), P())
    return jax.shard_map(
        body, mesh=mesh, in_specs=placed, out_specs=P("row", "col"), check_vma=False
    )
```

```python
import jax
import jax.numpy as jnp
from jax import lax
from jax.sharding import PartitionSpec as P

BASIS = 23
TILE = 128
TR = 2
STEPS = 14

AXES = ("row", "col")


def send(value, pairs):
    return lax.ppermute(value, AXES, pairs)


def mirror_pairs(row_count, col_count, flip):
    pairs = []
    for r in range(row_count):
        for c in range(col_count):
            half = (r % 2) ^ flip
            target = (2 * c + half, r // 2)
            pairs.append((r * col_count + c, target[0] * col_count + target[1]))
    return pairs


def shift(value, axis, by):
    length = lax.axis_size(axis)
    return lax.ppermute(value, axis, [(i, (i - by) % length) for i in range(length)])


def left_pairs(row_count, col_count, step):
    pairs = []
    for r in range(row_count):
        half = (r + step) % 2
        for c in range(col_count):
            target = ((2 * c + half - r - step) % row_count) // 2
            pairs.append((r * col_count + c, r * col_count + target))
    return pairs


def right_pairs(row_count, col_count, step):
    pairs = []
    for r in range(row_count):
        for c in range(col_count):
            target = (r - 2 * c - step) % row_count
            pairs.append((r * col_count + c, target * col_count + c))
    return pairs


def body(upper, occupied, tile_molecules):
    row_id = lax.axis_index("row")
    col_id = lax.axis_index("col")
    row_count = lax.axis_size("row")
    col_count = lax.axis_size("col")
    height = upper.shape[0]
    width = upper.shape[1]
    half_width = width // 2
    row_tiles = row_id * TR + jnp.arange(TR, dtype=jnp.int32)
    col_tiles = col_id * (2 * TR) + jnp.arange(2 * TR, dtype=jnp.int32)
    factor = jnp.where(
        row_tiles[:, None] < col_tiles[None, :],
        occupied.astype(jnp.float32),
        jnp.where(row_tiles[:, None] == col_tiles[None, :], 0.5, 0.0),
    )
    half_tri = (upper.reshape(TR, TILE, 2 * TR, TILE) * factor[:, None, :, None]).reshape(
        height, width
    )
    parity = row_id % 2
    halves = half_tri.reshape(height, 2, half_width)
    own_half = jnp.where(parity == 0, halves[:, 0], halves[:, 1]).T
    other_half = jnp.where(parity == 0, halves[:, 1], halves[:, 0]).T
    got_same = send(own_half, mirror_pairs(row_count, col_count, 0))
    got_other = send(other_half, mirror_pairs(row_count, col_count, 1))
    mirrored = jnp.where(
        parity == 0,
        jnp.concatenate([got_same, got_other], axis=1),
        jnp.concatenate([got_other, got_same], axis=1),
    )
    mol_rows = lax.dynamic_slice_in_dim(tile_molecules, row_id * TR, TR)
    mol_cols = lax.dynamic_slice_in_dim(tile_molecules, col_id * (2 * TR), 2 * TR)
    offsets = jnp.arange(TILE, dtype=jnp.int32)
    live_rows = (offsets[None, :] < BASIS * mol_rows[:, None]).astype(jnp.float32).reshape(height)
    live_cols = (offsets[None, :] < BASIS * mol_cols[:, None]).astype(jnp.float32).reshape(width)
    density = (half_tri + mirrored) * live_rows[:, None] * live_cols[None, :]
    group = upper.shape[0]
    row_panel = lax.all_gather(density, "col", axis=1, tiled=True)
    middle = STEPS // 2
    centre = send(density, right_pairs(row_count, col_count, middle))
    ahead = centre
    behind = centre
    after = []
    before = []
    for _ in range(STEPS - 1 - middle):
        ahead = shift(ahead, "row", 1)
        after.append(ahead)
    for _ in range(middle):
        behind = shift(behind, "row", -1)
        before.insert(0, behind)
    pieces = before + [centre] + after
    wrapped = jnp.concatenate([row_panel, row_panel[:, :group]], axis=1)
    total = None
    for step in range(0, STEPS, 2):
        start = (row_id + 2 * col_id + step) % row_count
        left = lax.dynamic_slice_in_dim(wrapped, start * group, 2 * group, axis=1)
        right = jnp.concatenate(pieces[step : step + 2], axis=0)
        term = jnp.dot(left, right, precision=lax.Precision.HIGHEST, preferred_element_type=jnp.float32)
        total = term if total is None else total + term
    return total


def solution(mesh):
    placed = (P("row", "col"), P("row", "col"), P())
    return jax.shard_map(
        body, mesh=mesh, in_specs=placed, out_specs=P("row", "col"), check_vma=False
    )
```

```python
import jax
import jax.numpy as jnp
from jax import lax
from jax.sharding import PartitionSpec as P

BASIS = 23
TILE = 128
TR = 2
STEPS = 14

AXES = ("row", "col")


def send(value, pairs):
    return lax.ppermute(value, AXES, pairs)


def mirror_pairs(row_count, col_count, flip):
    pairs = []
    for r in range(row_count):
        for c in range(col_count):
            half = (r % 2) ^ flip
            target = (2 * c + half, r // 2)
            pairs.append((r * col_count + c, target[0] * col_count + target[1]))
    return pairs


def shift(value, axis, by):
    length = lax.axis_size(axis)
    return lax.ppermute(value, axis, [(i, (i - by) % length) for i in range(length)])


def left_pairs(row_count, col_count, step):
    pairs = []
    for r in range(row_count):
        half = (r + step) % 2
        for c in range(col_count):
            target = ((2 * c + half - r - step) % row_count) // 2
            pairs.append((r * col_count + c, r * col_count + target))
    return pairs


def right_pairs(row_count, col_count, step):
    pairs = []
    for r in range(row_count):
        for c in range(col_count):
            target = (r - 2 * c - step) % row_count
            pairs.append((r * col_count + c, target * col_count + c))
    return pairs


def body(upper, occupied, tile_molecules):
    row_id = lax.axis_index("row")
    col_id = lax.axis_index("col")
    row_count = lax.axis_size("row")
    col_count = lax.axis_size("col")
    height = upper.shape[0]
    width = upper.shape[1]
    half_width = width // 2
    row_tiles = row_id * TR + jnp.arange(TR, dtype=jnp.int32)
    col_tiles = col_id * (2 * TR) + jnp.arange(2 * TR, dtype=jnp.int32)
    factor = jnp.where(
        row_tiles[:, None] < col_tiles[None, :],
        occupied.astype(jnp.float32),
        jnp.where(row_tiles[:, None] == col_tiles[None, :], 0.5, 0.0),
    )
    half_tri = (upper.reshape(TR, TILE, 2 * TR, TILE) * factor[:, None, :, None]).reshape(
        height, width
    )
    parity = row_id % 2
    halves = half_tri.reshape(height, 2, half_width)
    own_half = jnp.where(parity == 0, halves[:, 0], halves[:, 1]).T
    other_half = jnp.where(parity == 0, halves[:, 1], halves[:, 0]).T
    got_same = send(own_half, mirror_pairs(row_count, col_count, 0))
    got_other = send(other_half, mirror_pairs(row_count, col_count, 1))
    mirrored = jnp.where(
        parity == 0,
        jnp.concatenate([got_same, got_other], axis=1),
        jnp.concatenate([got_other, got_same], axis=1),
    )
    mol_rows = lax.dynamic_slice_in_dim(tile_molecules, row_id * TR, TR)
    mol_cols = lax.dynamic_slice_in_dim(tile_molecules, col_id * (2 * TR), 2 * TR)
    offsets = jnp.arange(TILE, dtype=jnp.int32)
    live_rows = (offsets[None, :] < BASIS * mol_rows[:, None]).astype(jnp.float32).reshape(height)
    live_cols = (offsets[None, :] < BASIS * mol_cols[:, None]).astype(jnp.float32).reshape(width)
    density = (half_tri + mirrored) * live_rows[:, None] * live_cols[None, :]
    group = upper.shape[0]
    row_panel = lax.all_gather(density, "col", axis=1, tiled=True)
    middle = STEPS // 2
    centre = send(density, right_pairs(row_count, col_count, middle))
    ahead = centre
    behind = centre
    after = []
    before = []
    for _ in range(STEPS - 1 - middle):
        ahead = shift(ahead, "row", 1)
        after.append(ahead)
    for _ in range(middle):
        behind = shift(behind, "row", -1)
        before.insert(0, behind)
    pieces = before + [centre] + after
    total = None
    for first in range(middle, STEPS):
        pair = (first, STEPS - 1 - first)
        lefts = []
        for step in pair:
            start = (row_id + 2 * col_id + step) % row_count
            lefts.append(lax.dynamic_slice_in_dim(row_panel, start * group, group, axis=1))
        left = jnp.concatenate(lefts, axis=1)
        right = jnp.concatenate([pieces[step] for step in pair], axis=0)
        term = jnp.dot(left, right, precision=lax.Precision.HIGHEST, preferred_element_type=jnp.float32)
        total = term if total is None else total + term
    return total


def solution(mesh):
    placed = (P("row", "col"), P("row", "col"), P())
    return jax.shard_map(
        body, mesh=mesh, in_specs=placed, out_specs=P("row", "col"), check_vma=False
    )
```
